32 devices in a mesh: groups: 2 (over y), seq: 16 (over z, x, core).
Axes of the slice: x: 2, y: 2, z: 4, core: 2. Of those that a mesh axis runs over, the one named last changes fastest.
Arguments:
- queries: bfloat16 [8192, 2048], P(('groups', 'seq')), parts along dimension 0, may hold values from -6 to 6
- keys: bfloat16 [8192, 2048], P(('groups', 'seq')), parts along dimension 0, may hold values from -6 to 6
- values: bfloat16 [8192, 2048], P(('groups', 'seq')), parts along dimension 0, may hold values from -6 to 6
Outputs:
- attended: bfloat16 [8192, 2048], P(('groups', 'seq')), parts along dimension 0
The draws below stay inside these ranges and needn't reach their ends.
There are 2 independent parts, one for each index of `groups`. The reference program is written for one: setup_inputs(seed, part) draws one part's arguments, and reference() takes and returns one part's arrays. A program takes and returns all parts, laid end to end along the dimension named above; each array names one. Nothing has to cross between parts.
All inputs are finite; a program needn't handle non-finite values.
Results may differ from the reference program's by a relative error of at most 0.0049.
Values may be sent and summed in bfloat16 or wider, within the bound.
No kernel may reach another device: no remote copies, remote signals or barrier semaphores. Data moves between devices by JAX's collectives and lax.ppermute only.
A program may use at most 256 MiB of HBM per device.

```python
import jax
import jax.numpy as jnp
from jax import lax

HEADS = 16
DK = 128
TOK_DEV = 256
TOKENS = 4096


def shard_levels(rng, extent, cuts, least, largest):
    factor_of = 1.0
    for dim, parts in cuts:
        draws = jax.random.uniform(jax.random.fold_in(jax.random.fold_in(rng, 6), dim), (parts,), jnp.float32, least / len(cuts), largest / len(cuts))
        factor_of = factor_of * jnp.repeat(jnp.exp(draws), extent[dim] // parts).reshape((-1,) + (1,) * (len(extent) - 1 - dim))
    return factor_of


def normal_values(own_key, shape, spread, bound, cuts=(), kind=jnp.bfloat16):
    drawn = jax.random.normal(own_key, shape, jnp.float32) * spread
    if len(cuts) > 0:
        drawn = shard_levels(own_key, shape, cuts, -0.22, 0.18) * drawn
    return jnp.clip(drawn, min=-bound, max=bound).astype(kind)


def setup_inputs(seed: int = 0, part: int = 0) -> dict:
    key_list = jax.random.split(jax.random.key(seed), 4)
    part_splits = jax.random.split(jax.random.fold_in(key_list[3], part), 4)
    return {
        "queries": normal_values(part_splits[0], (TOKENS, HEADS * DK), 1.0, 6.0, ((0, 16),)),
        "keys": normal_values(part_splits[1], (TOKENS, HEADS * DK), 1.0, 6.0, ((0, 16),)),
        "values": normal_values(part_splits[2], (TOKENS, HEADS * DK), 1.0, 6.0, ((0, 16),)),
    }


def reference(queries, keys, values):
    count = TOKENS // TOK_DEV
    q_all = queries.reshape(count, TOK_DEV, HEADS, DK)
    k_all = keys.reshape(count, TOK_DEV, HEADS, DK)
    v_all = values.reshape(count, TOK_DEV, HEADS, DK)
    scale = 1.0 / jnp.sqrt(jnp.float32(DK * TOKENS))
    rows = lax.broadcasted_iota(jnp.int32, (TOK_DEV, TOK_DEV), 0)
    cols = lax.broadcasted_iota(jnp.int32, (TOK_DEV, TOK_DEV), 1)
    causal = cols <= rows

    def step(state, block):
        q_blk, k_blk, v_blk = block
        qf = q_blk.astype(jnp.float32)
        kf = k_blk.astype(jnp.float32)
        vf = v_blk.astype(jnp.float32)
        scores = jnp.einsum('thd,shd->hts', qf, kf)
        scores = jnp.where(causal[None], scores, jnp.float32(0.0)).astype(jnp.bfloat16)
        intra = jnp.einsum('hts,she->the', scores.astype(jnp.float32), vf)
        carried = state.astype(jnp.bfloat16).astype(jnp.float32)
        inter = jnp.einsum('thd,hde->the', qf, carried)
        result = ((intra + inter) * scale).astype(jnp.bfloat16)
        state = state + jnp.einsum('thd,the->hde', kf, vf)
        return (state, result)
    start = jnp.zeros((HEADS, DK, DK), jnp.float32)
    final_state, outputs = lax.scan(step, start, (q_all, k_all, v_all))
    return outputs.reshape(TOKENS, HEADS * DK)
```

```python
import jax
import jax.numpy as jnp
from jax import lax
from jax.sharding import PartitionSpec as P

HEADS = 16
DK = 128


def on_device(queries, keys, values):
    tok = queries.shape[0]
    sources = lax.axis_size("seq")
    q_blk = queries.reshape(tok, HEADS, DK)
    k_blk = keys.reshape(tok, HEADS, DK)
    v_blk = values.reshape(tok, HEADS, DK)
    local_state = jnp.einsum("thd,the->hde", k_blk, v_blk, preferred_element_type=jnp.float32)
    flat = local_state.reshape(HEADS * DK, DK).astype(jnp.bfloat16)
    received = lax.all_to_all(flat, "seq", split_axis=0, concat_axis=0, tiled=True)
    received = received.reshape(sources, HEADS * DK // sources, DK)
    row_index = lax.broadcasted_iota(jnp.int32, (sources, sources), 0)
    col_index = lax.broadcasted_iota(jnp.int32, (sources, sources), 1)
    lower = (col_index < row_index).astype(jnp.bfloat16)
    earlier = jnp.einsum("cb,brd->crd", lower, received, preferred_element_type=jnp.float32)
    summed = lax.all_to_all(
        earlier.astype(jnp.bfloat16), "seq", split_axis=0, concat_axis=0, tiled=True
    )
    carried = summed.reshape(HEADS, DK, DK)
    rows = lax.broadcasted_iota(jnp.int32, (tok, tok), 0)
    cols = lax.broadcasted_iota(jnp.int32, (tok, tok), 1)
    causal = cols <= rows
    scores = jnp.einsum("thd,shd->hts", q_blk, k_blk, preferred_element_type=jnp.float32)
    scores = jnp.where(causal[None], scores, jnp.float32(0.0)).astype(jnp.bfloat16)
    intra = jnp.einsum("hts,she->the", scores, v_blk, preferred_element_type=jnp.float32)
    inter = jnp.einsum("thd,hde->the", q_blk, carried, preferred_element_type=jnp.float32)
    scale = 1.0 / jnp.sqrt(jnp.float32(DK * tok * sources))
    attended = ((intra + inter) * scale).astype(jnp.bfloat16)
    return attended.reshape(tok, HEADS * DK)


def solution(mesh):
    placed = (P(("groups", "seq"), None), P(("groups", "seq"), None), P(("groups", "seq"), None))
    return jax.shard_map(
        on_device, mesh=mesh, in_specs=placed, out_specs=P(("groups", "seq"), None), check_vma=False
    )
```

```python
import jax
import jax.numpy as jnp
from jax import lax
from jax.sharding import PartitionSpec as P

HEADS = 16
DK = 128


def on_device(queries, keys, values):
    tok = queries.shape[0]
    sources = lax.axis_size("seq")
    q_blk = queries.reshape(tok, HEADS, DK)
    k_blk = keys.reshape(tok, HEADS, DK)
    v_blk = values.reshape(tok, HEADS, DK)
    local_state = jnp.einsum("thd,the->hde", k_blk, v_blk, preferred_element_type=jnp.float32)
    flat = local_state.reshape(HEADS * DK, DK).astype(jnp.float16)
    received = lax.all_to_all(flat, "seq", split_axis=0, concat_axis=0, tiled=True)
    received = received.reshape(sources, HEADS * DK // sources, DK)
    row_index = lax.broadcasted_iota(jnp.int32, (sources, sources), 0)
    col_index = lax.broadcasted_iota(jnp.int32, (sources, sources), 1)
    lower = (col_index < row_index).astype(jnp.float32)
    earlier = jnp.einsum(
        "cb,brd->crd",
        lower,
        received.astype(jnp.float32),
        precision=lax.Precision.HIGHEST,
        preferred_element_type=jnp.float32,
    )
    summed = lax.all_to_all(
        earlier.astype(jnp.bfloat16), "seq", split_axis=0, concat_axis=0, tiled=True
    )
    carried = summed.reshape(HEADS, DK, DK)
    rows = lax.broadcasted_iota(jnp.int32, (tok, tok), 0)
    cols = lax.broadcasted_iota(jnp.int32, (tok, tok), 1)
    causal = cols <= rows
    scores = jnp.einsum("thd,shd->hts", q_blk, k_blk, preferred_element_type=jnp.float32)
    scores = jnp.where(causal[None], scores, jnp.float32(0.0)).astype(jnp.bfloat16)
    intra = jnp.einsum("hts,she->the", scores, v_blk, preferred_element_type=jnp.float32)
    inter = jnp.einsum("thd,hde->the", q_blk, carried, preferred_element_type=jnp.float32)
    scale = 1.0 / jnp.sqrt(jnp.float32(DK * tok * sources))
    attended = ((intra + inter) * scale).astype(jnp.bfloat16)
    return attended.reshape(tok, HEADS * DK)


def solution(mesh):
    placed = (P(("groups", "seq"), None), P(("groups", "seq"), None), P(("groups", "seq"), None))
    return jax.shard_map(
        on_device, mesh=mesh, in_specs=placed, out_specs=P(("groups", "seq"), None), check_vma=False
    )
```

```python
import functools

import jax
import numpy as np
import jax.numpy as jnp
from jax import lax
from jax.experimental import pallas as pl
from jax.experimental.pallas import tpu as pltpu
from jax.sharding import PartitionSpec as P

HEADS = 16
DK = 128
GROUP = 4


def state_kernel(k_ref, v_ref, o_ref):
    for j in range(GROUP):
        cols = slice(j * DK, (j + 1) * DK)
        s = lax.dot_general(
            k_ref[:, cols], v_ref[:, cols], (((0,), (0,)), ((), ())),
            preferred_element_type=jnp.float32,
        )
        o_ref[j * DK:(j + 1) * DK, :] = s.astype(o_ref.dtype)


def intra_kernel(q_ref, k_ref, v_ref, o_ref):
    tok = q_ref.shape[0]
    rows = lax.broadcasted_iota(jnp.int32, (tok, tok), 0)
    cols_i = lax.broadcasted_iota(jnp.int32, (tok, tok), 1)
    causal = cols_i <= rows
    for j in range(GROUP):
        cols = slice(j * DK, (j + 1) * DK)
        s = lax.dot_general(
            q_ref[:, cols], k_ref[:, cols], (((1,), (1,)), ((), ())),
            preferred_element_type=jnp.float32,
        )
        s = jnp.where(causal, s, jnp.float32(0.0)).astype(jnp.bfloat16)
        o_ref[:, cols] = jnp.dot(s, v_ref[:, cols], preferred_element_type=jnp.float32)


def final_kernel(scale, q_ref, p_ref, intra_ref, o_ref):
    for j in range(GROUP):
        cols = slice(j * DK, (j + 1) * DK)
        inter = jnp.dot(q_ref[:, cols], p_ref[j * DK:(j + 1) * DK, :], preferred_element_type=jnp.float32)
        o_ref[:, cols] = ((intra_ref[:, cols] + inter) * scale).astype(o_ref.dtype)


def local_states(keys, values):
    tok = keys.shape[0]
    steps = HEADS // GROUP
    return pl.pallas_call(
        state_kernel,
        grid=(steps,),
        in_specs=[pl.BlockSpec((tok, GROUP * DK), lambda i: (0, i))] * 2,
        out_specs=pl.BlockSpec((GROUP * DK, DK), lambda i: (i, 0)),
        out_shape=jax.ShapeDtypeStruct((HEADS * DK, DK), jnp.float32),
        cost_estimate=pl.CostEstimate(
            flops=2 * tok * DK * DK * HEADS, transcendentals=0,
            bytes_accessed=2 * tok * HEADS * DK * 2 + HEADS * DK * DK * 4,
        ),
    )(keys, values)


def intra_block(queries, keys, values):
    tok = queries.shape[0]
    steps = HEADS // GROUP
    spec = pl.BlockSpec((tok, GROUP * DK), lambda i: (0, i))
    return pl.pallas_call(
        intra_kernel,
        grid=(steps,),
        in_specs=[spec] * 3,
        out_specs=spec,
        out_shape=jax.ShapeDtypeStruct((tok, HEADS * DK), jnp.float32),
        cost_estimate=pl.CostEstimate(
            flops=4 * tok * tok * DK * HEADS, transcendentals=0,
            bytes_accessed=3 * tok * HEADS * DK * 2 + tok * HEADS * DK * 4,
        ),
    )(queries, keys, values)


def combine(queries, carried, intra, scale):
    tok = queries.shape[0]
    steps = HEADS // GROUP
    spec = pl.BlockSpec((tok, GROUP * DK), lambda i: (0, i))
    return pl.pallas_call(
        functools.partial(final_kernel, scale),
        grid=(steps,),
        in_specs=[spec, pl.BlockSpec((GROUP * DK, DK), lambda i: (i, 0)), spec],
        out_specs=spec,
        out_shape=jax.ShapeDtypeStruct((tok, HEADS * DK), jnp.bfloat16),
        cost_estimate=pl.CostEstimate(
            flops=2 * tok * DK * DK * HEADS, transcendentals=0,
            bytes_accessed=2 * tok * HEADS * DK * 2 + tok * HEADS * DK * 4 + HEADS * DK * DK * 2,
        ),
    )(queries, carried, intra)


def on_device(queries, keys, values):
    tok = queries.shape[0]
    sources = lax.axis_size("seq")
    flat = local_states(keys, values).astype(jnp.float16)
    received = lax.all_to_all(flat, "seq", split_axis=0, concat_axis=0, tiled=True)
    received = received.reshape(sources, HEADS * DK // sources, DK)
    row_index = lax.broadcasted_iota(jnp.int32, (sources, sources), 0)
    col_index = lax.broadcasted_iota(jnp.int32, (sources, sources), 1)
    lower = (col_index < row_index).astype(jnp.float32)
    earlier = jnp.einsum(
        "cb,brd->crd",
        lower,
        received.astype(jnp.float32),
        precision=lax.Precision.HIGHEST,
        preferred_element_type=jnp.float32,
    )
    summed = lax.all_to_all(
        earlier.astype(jnp.bfloat16), "seq", split_axis=0, concat_axis=0, tiled=True
    )
    carried = summed.reshape(HEADS * DK, DK)
    intra = intra_block(queries, keys, values)
    scale = float(np.float32(1.0) / np.sqrt(np.float32(DK * tok * sources)))
    return combine(queries, carried, intra, scale)


def solution(mesh):
    placed = (P(("groups", "seq"), None), P(("groups", "seq"), None), P(("groups", "seq"), None))
    return jax.shard_map(
        on_device, mesh=mesh, in_specs=placed, out_specs=P(("groups", "seq"), None), check_vma=False
    )
```

```python
import jax
import jax.numpy as jnp
from jax import lax
from jax.sharding import PartitionSpec as P

HEADS = 16
DK = 128


def on_device(queries, keys, values):
    tok = queries.shape[0]
    sources = lax.axis_size("seq")
    q_blk = queries.reshape(tok, HEADS, DK)
    k_blk = keys.reshape(tok, HEADS, DK)
    v_blk = values.reshape(tok, HEADS, DK)
    local_state = jnp.einsum("thd,the->hde", k_blk, v_blk, preferred_element_type=jnp.float32)
    flat = local_state.reshape(HEADS * DK, DK).astype(jnp.float16)
    received = lax.all_to_all(flat, "seq", split_axis=0, concat_axis=0, tiled=True)
    received = received.reshape(sources, HEADS * DK // sources, DK)
    received = received.astype(jnp.float32)
    running = jnp.zeros_like(received[0])
    prefixes = []
    for source in range(sources):
        prefixes.append(running)
        running = running + received[source]
    earlier = jnp.stack(prefixes)
    summed = lax.all_to_all(
        earlier.astype(jnp.bfloat16), "seq", split_axis=0, concat_axis=0, tiled=True
    )
    carried = summed.reshape(HEADS, DK, DK)
    rows = lax.broadcasted_iota(jnp.int32, (tok, tok), 0)
    cols = lax.broadcasted_iota(jnp.int32, (tok, tok), 1)
    causal = cols <= rows
    scores = jnp.einsum("thd,shd->hts", q_blk, k_blk, preferred_element_type=jnp.float32)
    scores = jnp.where(causal[None], scores, jnp.float32(0.0)).astype(jnp.bfloat16)
    intra = jnp.einsum("hts,she->the", scores, v_blk, preferred_element_type=jnp.float32)
    inter = jnp.einsum("thd,hde->the", q_blk, carried, preferred_element_type=jnp.float32)
    scale = 1.0 / jnp.sqrt(jnp.float32(DK * tok * sources))
    attended = ((intra + inter) * scale).astype(jnp.bfloat16)
    return attended.reshape(tok, HEADS * DK)


def solution(mesh):
    placed = (P(("groups", "seq"), None), P(("groups", "seq"), None), P(("groups", "seq"), None))
    return jax.shard_map(
        on_device, mesh=mesh, in_specs=placed, out_specs=P(("groups", "seq"), None), check_vma=False
    )
```

```python
import jax
import jax.numpy as jnp
from jax import lax
from jax.sharding import PartitionSpec as P

HEADS = 16
DK = 128


def on_device(queries, keys, values):
    tok = queries.shape[0]
    sources = lax.axis_size("seq")
    q_blk = queries.reshape(tok, HEADS, DK)
    k_blk = keys.reshape(tok, HEADS, DK)
    v_blk = values.reshape(tok, HEADS, DK)
    local_state = jnp.einsum("the,thd->hed", v_blk, k_blk, preferred_element_type=jnp.float32)
    flat = local_state.reshape(HEADS * DK, DK).astype(jnp.float16)
    received = lax.all_to_all(flat, "seq", split_axis=0, concat_axis=0, tiled=True)
    received = received.reshape(sources, HEADS * DK // sources, DK)
    widened = received.astype(jnp.float32)
    earlier = jnp.cumsum(widened, axis=0) - widened
    summed = lax.all_to_all(
        earlier.astype(jnp.bfloat16), "seq", split_axis=0, concat_axis=0, tiled=True
    )
    carried = summed.reshape(HEADS, DK, DK)
    rows = lax.broadcasted_iota(jnp.int32, (tok, tok), 0)
    cols = lax.broadcasted_iota(jnp.int32, (tok, tok), 1)
    causal = cols <= rows
    scores = jnp.einsum("thd,shd->hts", q_blk, k_blk, preferred_element_type=jnp.float32)
    scores = jnp.where(causal[None], scores, jnp.float32(0.0)).astype(jnp.bfloat16)
    intra = jnp.einsum("hts,she->the", scores, v_blk, preferred_element_type=jnp.float32)
    inter = jnp.einsum("thd,hed->the", q_blk, carried, preferred_element_type=jnp.float32)
    scale = 1.0 / jnp.sqrt(jnp.float32(DK * tok * sources))
    attended = ((intra + inter) * scale).astype(jnp.bfloat16)
    return attended.reshape(tok, HEADS * DK)


def solution(mesh):
    placed = (P(("groups", "seq"), None), P(("groups", "seq"), None), P(("groups", "seq"), None))
    return jax.shard_map(
        on_device, mesh=mesh, in_specs=placed, out_specs=P(("groups", "seq"), None), check_vma=False
    )
```

```python
import functools

import jax
import numpy as np
import jax.numpy as jnp
from jax import lax
from jax.experimental import pallas as pl
from jax.experimental.pallas import tpu as pltpu
from jax.sharding import PartitionSpec as P

HEADS = 16
DK = 128
GROUP = 8


def intra_kernel(q_ref, k_ref, v_ref, o_ref):
    tok = q_ref.shape[0]
    rows = lax.broadcasted_iota(jnp.int32, (tok, tok), 0)
    cols_i = lax.broadcasted_iota(jnp.int32, (tok, tok), 1)
    causal = cols_i <= rows
    for j in range(GROUP):
        cols = slice(j * DK, (j + 1) * DK)
        s = lax.dot_general(
            q_ref[:, cols], k_ref[:, cols], (((1,), (1,)), ((), ())),
            preferred_element_type=jnp.float32,
        )
        s = jnp.where(causal, s, jnp.float32(0.0)).astype(jnp.bfloat16)
        o_ref[:, cols] = jnp.dot(s, v_ref[:, cols], preferred_element_type=jnp.float32)


def final_kernel(scale, q_ref, p_ref, intra_ref, o_ref):
    base = pl.program_id(0) * (GROUP * DK)
    for j in range(GROUP):
        cols = slice(j * DK, (j + 1) * DK)
        start = pl.multiple_of(base + j * DK, DK)
        inter = lax.dot_general(
            q_ref[:, cols], p_ref[pl.ds(start, DK), :], (((1,), (1,)), ((), ())),
            preferred_element_type=jnp.float32,
        )
        o_ref[:, cols] = ((intra_ref[:, cols] + inter) * scale).astype(o_ref.dtype)


def intra_block(queries, keys, values):
    tok = queries.shape[0]
    spec = pl.BlockSpec((tok, GROUP * DK), lambda i: (0, i))
    return pl.pallas_call(
        intra_kernel,
        grid=(HEADS // GROUP,),
        in_specs=[spec] * 3,
        out_specs=spec,
        out_shape=jax.ShapeDtypeStruct((tok, HEADS * DK), jnp.float32),
        cost_estimate=pl.CostEstimate(
            flops=4 * tok * tok * DK * HEADS, transcendentals=0,
            bytes_accessed=3 * tok * HEADS * DK * 2 + tok * HEADS * DK * 4,
        ),
    )(queries, keys, values)


def combine(queries, carried_t, intra, scale):
    tok = queries.shape[0]
    spec = pl.BlockSpec((tok, GROUP * DK), lambda i: (0, i))
    return pl.pallas_call(
        functools.partial(final_kernel, scale),
        grid=(HEADS // GROUP,),
        in_specs=[spec, pl.BlockSpec(memory_space=pltpu.VMEM), spec],
        out_specs=spec,
        out_shape=jax.ShapeDtypeStruct((tok, HEADS * DK), jnp.bfloat16),
        cost_estimate=pl.CostEstimate(
            flops=2 * tok * DK * DK * HEADS, transcendentals=0,
            bytes_accessed=2 * tok * HEADS * DK * 2 + tok * HEADS * DK * 4 + HEADS * DK * DK * 2,
        ),
    )(queries, carried_t, intra)


def on_device(queries, keys, values):
    tok = queries.shape[0]
    sources = lax.axis_size("seq")
    q_blk = queries.reshape(tok, HEADS, DK)
    k_blk = keys.reshape(tok, HEADS, DK)
    v_blk = values.reshape(tok, HEADS, DK)
    local_state = jnp.einsum("the,thd->hed", v_blk, k_blk, preferred_element_type=jnp.float32)
    flat = local_state.reshape(HEADS * DK, DK).astype(jnp.float16)
    received = lax.all_to_all(flat, "seq", split_axis=0, concat_axis=0, tiled=True)
    received = received.reshape(sources, HEADS * DK // sources, DK)
    widened = received.astype(jnp.float32)
    earlier = jnp.cumsum(widened, axis=0) - widened
    summed = lax.all_to_all(
        earlier.astype(jnp.bfloat16), "seq", split_axis=0, concat_axis=0, tiled=True
    )
    carried_t = summed.reshape(HEADS * DK, DK)
    intra = intra_block(queries, keys, values)
    scale = float(np.float32(1.0) / np.sqrt(np.float32(DK * tok * sources)))
    return combine(queries, carried_t, intra, scale)

def solution(mesh):
    placed = (P(("groups", "seq"), None), P(("groups", "seq"), None), P(("groups", "seq"), None))
    return jax.shard_map(
        on_device, mesh=mesh, in_specs=placed, out_specs=P(("groups", "seq"), None), check_vma=False
    )
```

```python
import math

import jax
import jax.numpy as jnp
import numpy as np
from jax import lax
from jax.sharding import Mesh
from jax.sharding import PartitionSpec as P

HEADS = 16
DK = 128
LIMIT = 6.0
F16_MAX = 65504.0


def swap_cores(x):
    return lax.ppermute(x, "core", [(0, 1), (1, 0)])


def on_device(queries, keys, values):
    tok = queries.shape[0]
    chips = lax.axis_size("chip")
    core = lax.axis_index("core")
    sources = chips * lax.axis_size("core")
    q_blk = queries.reshape(tok, HEADS, DK)
    k_blk = keys.reshape(tok, HEADS, DK)
    v_blk = values.reshape(tok, HEADS, DK)
    local_state = jnp.einsum("the,thd->hed", v_blk, k_blk, preferred_element_type=jnp.float32)
    flat = local_state.reshape(HEADS * DK, DK)
    half = HEADS * DK // 2
    own = lax.dynamic_slice_in_dim(flat, core * half, half)
    other = lax.dynamic_slice_in_dim(flat, (1 - core) * half, half)
    partner = swap_cores(other)
    chip_sum = own + partner
    received = lax.all_to_all(chip_sum.astype(jnp.float16), "chip", split_axis=0, concat_axis=0, tiled=True)
    received = received.reshape(chips, half // chips, DK).astype(jnp.float32)
    earlier = jnp.cumsum(received, axis=0) - received
    bound = (chips - 1) * 2 * tok * LIMIT * LIMIT
    shift = max(0, math.ceil(math.log2(bound / F16_MAX)))
    down = np.float32(2.0 ** -shift)
    back = lax.all_to_all((earlier * down).astype(jnp.float16), "chip", split_axis=0, concat_axis=0, tiled=True)
    chip_prefix = back.reshape(half, DK).astype(jnp.float32) * np.float32(2.0 ** shift)
    first = core == 0
    kept = (chip_prefix + jnp.where(first, jnp.float32(0.0), partner)).astype(jnp.bfloat16)
    sent = (chip_prefix + jnp.where(first, own, jnp.float32(0.0))).astype(jnp.bfloat16)
    got = swap_cores(sent)
    low = jnp.where(first, kept, got)
    high = jnp.where(first, got, kept)
    carried = jnp.concatenate([low, high], axis=0).reshape(HEADS, DK, DK)
    rows = lax.broadcasted_iota(jnp.int32, (tok, tok), 0)
    cols = lax.broadcasted_iota(jnp.int32, (tok, tok), 1)
    causal = cols <= rows
    scores = jnp.einsum("thd,shd->hts", q_blk, k_blk, preferred_element_type=jnp.float32)
    scores = jnp.where(causal[None], scores, jnp.float32(0.0)).astype(jnp.bfloat16)
    intra = jnp.einsum("hts,she->the", scores, v_blk, preferred_element_type=jnp.float32)
    inter = jnp.einsum("thd,hed->the", q_blk, carried, preferred_element_type=jnp.float32)
    scale = 1.0 / jnp.sqrt(jnp.float32(DK * tok * sources))
    attended = ((intra + inter) * scale).astype(jnp.bfloat16)
    return attended.reshape(tok, HEADS * DK)


def solution(mesh):
    devices = mesh.devices
    split = Mesh(devices.reshape(devices.shape[0], devices.shape[1] // 2, 2), ("groups", "chip", "core"))
    spec = P(("groups", "chip", "core"), None)
    return jax.shard_map(
        on_device, mesh=split, in_specs=(spec, spec, spec), out_specs=spec, check_vma=False
    )
```

```python
import math

import jax
import jax.numpy as jnp
import numpy as np
from jax import lax
from jax.sharding import Mesh
from jax.sharding import PartitionSpec as P

HEADS = 16
DK = 128
LIMIT = 6.0
F16_MAX = 65504.0


def swap_cores(x):
    return lax.ppermute(x, "core", [(0, 1), (1, 0)])


def on_device(queries, keys, values):
    tok = queries.shape[0]
    chips = lax.axis_size("chip")
    core = lax.axis_index("core")
    sources = chips * lax.axis_size("core")
    q_blk = queries.reshape(tok, HEADS, DK)
    k_blk = keys.reshape(tok, HEADS, DK)
    v_blk = values.reshape(tok, HEADS, DK)
    local_state = jnp.einsum("the,thd->hed", v_blk, k_blk, preferred_element_type=jnp.float32)
    flat = local_state.reshape(HEADS * DK, DK)
    half = HEADS * DK // 2
    own = lax.dynamic_slice_in_dim(flat, core * half, half)
    other = lax.dynamic_slice_in_dim(flat, (1 - core) * half, half)
    partner = swap_cores(other)
    chip_sum = own + partner
    received = lax.all_to_all(chip_sum.astype(jnp.float16), "chip", split_axis=0, concat_axis=0, tiled=True)
    received = received.reshape(chips, half // chips, DK).astype(jnp.float32)
    earlier = jnp.cumsum(received, axis=0) - received
    bound = (chips - 1) * 2 * tok * LIMIT * LIMIT
    shift = max(0, math.ceil(math.log2(bound / F16_MAX)))
    down = np.float32(2.0 ** -shift)
    back = lax.all_to_all((earlier * down).astype(jnp.float16), "chip", split_axis=0, concat_axis=0, tiled=True)
    chip_prefix = back.reshape(half, DK).astype(jnp.float32) * np.float32(2.0 ** shift)
    first = core == 0
    kept = (chip_prefix + jnp.where(first, jnp.float32(0.0), partner)).astype(jnp.bfloat16)
    sent = (chip_prefix + jnp.where(first, own, jnp.float32(0.0))).astype(jnp.bfloat16)
    rows = lax.broadcasted_iota(jnp.int32, (tok, tok), 0)
    cols = lax.broadcasted_iota(jnp.int32, (tok, tok), 1)
    causal = cols <= rows
    scores = jnp.einsum("thd,shd->hts", q_blk, k_blk, preferred_element_type=jnp.float32)
    scores = jnp.where(causal[None], scores, jnp.float32(0.0)).astype(jnp.bfloat16)
    intra = jnp.einsum("hts,she->the", scores, v_blk, preferred_element_type=jnp.float32)
    sent, intra = lax.optimization_barrier((sent, intra))
    got = swap_cores(sent)
    low = jnp.where(first, kept, got)
    high = jnp.where(first, got, kept)
    carried = jnp.concatenate([low, high], axis=0).reshape(HEADS, DK, DK)
    inter = jnp.einsum("thd,hed->the", q_blk, carried, preferred_element_type=jnp.float32)
    scale = 1.0 / jnp.sqrt(jnp.float32(DK * tok * sources))
    attended = ((intra + inter) * scale).astype(jnp.bfloat16)
    return attended.reshape(tok, HEADS * DK)


def solution(mesh):
    devices = mesh.devices
    split = Mesh(devices.reshape(devices.shape[0], devices.shape[1] // 2, 2), ("groups", "chip", "core"))
    spec = P(("groups", "chip", "core"), None)
    return jax.shard_map(
        on_device, mesh=split, in_specs=(spec, spec, spec), out_specs=spec, check_vma=False
    )
```

```python
import math

import jax
import jax.numpy as jnp
import numpy as np
from jax import lax
from jax.sharding import Mesh
from jax.sharding import PartitionSpec as P

HEADS = 16
DK = 128
LIMIT = 6.0
F16_MAX = 65504.0


def swap_cores(x):
    return lax.ppermute(x, "core", [(0, 1), (1, 0)])


def on_device(queries, keys, values):
    tok = queries.shape[0]
    chips = lax.axis_size("chip")
    core = lax.axis_index("core")
    sources = chips * lax.axis_size("core")
    q_blk = queries.reshape(tok, HEADS, DK)
    k_blk = keys.reshape(tok, HEADS, DK)
    v_blk = values.reshape(tok, HEADS, DK)
    half = HEADS * DK // 2

    def half_state(index):
        k_half = lax.dynamic_slice_in_dim(keys, index * half, half, axis=1).reshape(tok, HEADS // 2, DK)
        v_half = lax.dynamic_slice_in_dim(values, index * half, half, axis=1).reshape(tok, HEADS // 2, DK)
        state = jnp.einsum("the,thd->hed", v_half, k_half, preferred_element_type=jnp.float32)
        return state.reshape(half, DK)

    partner = swap_cores(half_state(1 - core))
    own = half_state(core)
    chip_sum = own + partner
    received = lax.all_to_all(chip_sum.astype(jnp.float16), "chip", split_axis=0, concat_axis=0, tiled=True)
    received = received.reshape(chips, half // chips, DK).astype(jnp.float32)
    earlier = jnp.cumsum(received, axis=0) - received
    bound = (chips - 1) * 2 * tok * LIMIT * LIMIT
    shift = max(0, math.ceil(math.log2(bound / F16_MAX)))
    down = np.float32(2.0 ** -shift)
    back = lax.all_to_all((earlier * down).astype(jnp.float16), "chip", split_axis=0, concat_axis=0, tiled=True)
    chip_prefix = back.reshape(half, DK).astype(jnp.float32) * np.float32(2.0 ** shift)
    first = core == 0
    kept = (chip_prefix + jnp.where(first, jnp.float32(0.0), partner)).astype(jnp.bfloat16)
    sent = (chip_prefix + jnp.where(first, own, jnp.float32(0.0))).astype(jnp.bfloat16)
    rows = lax.broadcasted_iota(jnp.int32, (tok, tok), 0)
    cols = lax.broadcasted_iota(jnp.int32, (tok, tok), 1)
    causal = cols <= rows
    scores = jnp.einsum("thd,shd->hts", q_blk, k_blk, preferred_element_type=jnp.float32)
    scores = jnp.where(causal[None], scores, jnp.float32(0.0)).astype(jnp.bfloat16)
    intra = jnp.einsum("hts,she->the", scores, v_blk, preferred_element_type=jnp.float32)
    sent, intra = lax.optimization_barrier((sent, intra))
    got = swap_cores(sent)
    low = jnp.where(first, kept, got)
    high = jnp.where(first, got, kept)
    carried = jnp.concatenate([low, high], axis=0).reshape(HEADS, DK, DK)
    inter = jnp.einsum("thd,hed->the", q_blk, carried, preferred_element_type=jnp.float32)
    scale = 1.0 / jnp.sqrt(jnp.float32(DK * tok * sources))
    attended = ((intra + inter) * scale).astype(jnp.bfloat16)
    return attended.reshape(tok, HEADS * DK)


def solution(mesh):
    devices = mesh.devices
    split = Mesh(devices.reshape(devices.shape[0], devices.shape[1] // 2, 2), ("groups", "chip", "core"))
    spec = P(("groups", "chip", "core"), None)
    return jax.shard_map(
        on_device, mesh=split, in_specs=(spec, spec, spec), out_specs=spec, check_vma=False
    )
```

```python
import math

import jax
import jax.numpy as jnp
import numpy as np
from jax import lax
from jax.sharding import Mesh
from jax.sharding import PartitionSpec as P

HEADS = 16
DK = 128
LIMIT = 6.0
F16_MAX = 65504.0


def swap_cores(x):
    return lax.ppermute(x, "core", [(0, 1), (1, 0)])


def on_device(queries, keys, values):
    tok = queries.shape[0]
    chips = lax.axis_size("chip")
    core = lax.axis_index("core")
    sources = chips * lax.axis_size("core")
    q_blk = queries.reshape(tok, HEADS, DK)
    k_blk = keys.reshape(tok, HEADS, DK)
    v_blk = values.reshape(tok, HEADS, DK)
    local_state = jnp.einsum("the,thd->hed", v_blk, k_blk, preferred_element_type=jnp.float32)
    flat = local_state.reshape(HEADS * DK, DK)
    half = HEADS * DK // 2
    partner_all = swap_cores(flat.astype(jnp.float16))
    own = lax.dynamic_slice_in_dim(flat, core * half, half)
    partner = lax.dynamic_slice_in_dim(partner_all, core * half, half).astype(jnp.float32)
    chip_sum = own + partner
    received = lax.all_to_all(chip_sum.astype(jnp.float16), "chip", split_axis=0, concat_axis=0, tiled=True)
    received = received.reshape(chips, half // chips, DK).astype(jnp.float32)
    earlier = jnp.cumsum(received, axis=0) - received
    bound = (chips - 1) * 2 * tok * LIMIT * LIMIT
    shift = max(0, math.ceil(math.log2(bound / F16_MAX)))
    down = np.float32(2.0 ** -shift)
    back = lax.all_to_all((earlier * down).astype(jnp.float16), "chip", split_axis=0, concat_axis=0, tiled=True)
    chip_prefix = back.reshape(half, DK).astype(jnp.float32) * np.float32(2.0 ** shift)
    first = core == 0
    kept = (chip_prefix + jnp.where(first, jnp.float32(0.0), partner)).astype(jnp.bfloat16)
    sent = (chip_prefix + jnp.where(first, own, jnp.float32(0.0))).astype(jnp.bfloat16)
    rows = lax.broadcasted_iota(jnp.int32, (tok, tok), 0)
    cols = lax.broadcasted_iota(jnp.int32, (tok, tok), 1)
    causal = cols <= rows
    scores = jnp.einsum("thd,shd->hts", q_blk, k_blk, preferred_element_type=jnp.float32)
    scores = jnp.where(causal[None], scores, jnp.float32(0.0)).astype(jnp.bfloat16)
    intra = jnp.einsum("hts,she->the", scores, v_blk, preferred_element_type=jnp.float32)
    sent, intra = lax.optimization_barrier((sent, intra))
    got = swap_cores(sent)
    low = jnp.where(first, kept, got)
    high = jnp.where(first, got, kept)
    carried = jnp.concatenate([low, high], axis=0).reshape(HEADS, DK, DK)
    inter = jnp.einsum("thd,hed->the", q_blk, carried, preferred_element_type=jnp.float32)
    scale = 1.0 / jnp.sqrt(jnp.float32(DK * tok * sources))
    attended = ((intra + inter) * scale).astype(jnp.bfloat16)
    return attended.reshape(tok, HEADS * DK)


def solution(mesh):
    devices = mesh.devices
    split = Mesh(devices.reshape(devices.shape[0], devices.shape[1] // 2, 2), ("groups", "chip", "core"))
    spec = P(("groups", "chip", "core"), None)
    return jax.shard_map(
        on_device, mesh=split, in_specs=(spec, spec, spec), out_specs=spec, check_vma=False
    )
```

```python
import math

import jax
import jax.numpy as jnp
import numpy as np
from jax import lax
from jax.sharding import Mesh
from jax.sharding import PartitionSpec as P

HEADS = 16
DK = 128
LIMIT = 6.0
F16_MAX = 65504.0


def swap_cores(x):
    return lax.ppermute(x, "core", [(0, 1), (1, 0)])


def on_device(queries, keys, values):
    tok = queries.shape[0]
    chips = lax.axis_size("chip")
    core = lax.axis_index("core")
    sources = chips * lax.axis_size("core")
    q_blk = queries.reshape(tok, HEADS, DK)
    k_blk = keys.reshape(tok, HEADS, DK)
    v_blk = values.reshape(tok, HEADS, DK)
    local_state = jnp.einsum("the,thd->hed", v_blk, k_blk, preferred_element_type=jnp.float32)
    flat = local_state.reshape(HEADS * DK, DK).astype(jnp.float16)
    half = HEADS * DK // 2
    partner_all = swap_cores(flat)
    own = lax.dynamic_slice_in_dim(flat, core * half, half).astype(jnp.float32)
    partner = lax.dynamic_slice_in_dim(partner_all, core * half, half).astype(jnp.float32)
    chip_sum = own + partner
    received = lax.all_to_all(chip_sum.astype(jnp.float16), "chip", split_axis=0, concat_axis=0, tiled=True)
    received = received.reshape(chips, half // chips, DK).astype(jnp.float32)
    earlier = jnp.cumsum(received, axis=0) - received
    bound = (chips - 1) * 2 * tok * LIMIT * LIMIT
    shift = max(0, math.ceil(math.log2(bound / F16_MAX)))
    down = np.float32(2.0 ** -shift)
    back = lax.all_to_all((earlier * down).astype(jnp.float16), "chip", split_axis=0, concat_axis=0, tiled=True)
    chip_prefix = back.reshape(half, DK).astype(jnp.float32) * np.float32(2.0 ** shift)
    first = core == 0
    kept = (chip_prefix + jnp.where(first, jnp.float32(0.0), partner)).astype(jnp.bfloat16)
    sent = (chip_prefix + jnp.where(first, own, jnp.float32(0.0))).astype(jnp.bfloat16)
    rows = lax.broadcasted_iota(jnp.int32, (tok, tok), 0)
    cols = lax.broadcasted_iota(jnp.int32, (tok, tok), 1)
    causal = cols <= rows
    scores = jnp.einsum("thd,shd->hts", q_blk, k_blk, preferred_element_type=jnp.float32)
    scores = jnp.where(causal[None], scores, jnp.float32(0.0)).astype(jnp.bfloat16)
    intra = jnp.einsum("hts,she->the", scores, v_blk, preferred_element_type=jnp.float32)
    sent, intra = lax.optimization_barrier((sent, intra))
    got = swap_cores(sent)
    low = jnp.where(first, kept, got)
    high = jnp.where(first, got, kept)
    carried = jnp.concatenate([low, high], axis=0).reshape(HEADS, DK, DK)
    inter = jnp.einsum("thd,hed->the", q_blk, carried, preferred_element_type=jnp.float32)
    scale = 1.0 / jnp.sqrt(jnp.float32(DK * tok * sources))
    attended = ((intra + inter) * scale).astype(jnp.bfloat16)
    return attended.reshape(tok, HEADS * DK)


def solution(mesh):
    devices = mesh.devices
    split = Mesh(devices.reshape(devices.shape[0], devices.shape[1] // 2, 2), ("groups", "chip", "core"))
    spec = P(("groups", "chip", "core"), None)
    return jax.shard_map(
        on_device, mesh=split, in_specs=(spec, spec, spec), out_specs=spec, check_vma=False
    )
```

```python
import math

import jax
import jax.numpy as jnp
import numpy as np
from jax import lax
from jax.sharding import Mesh
from jax.sharding import PartitionSpec as P

HEADS = 16
DK = 128
LIMIT = 6.0
F16_MAX = 65504.0


def swap_cores(x):
    return lax.ppermute(x, "core", [(0, 1), (1, 0)])


def on_device(queries, keys, values):
    tok = queries.shape[0]
    chips = lax.axis_size("chip")
    core = lax.axis_index("core")
    sources = chips * lax.axis_size("core")
    q_blk = queries.reshape(tok, HEADS, DK)
    k_blk = keys.reshape(tok, HEADS, DK)
    v_blk = values.reshape(tok, HEADS, DK)
    local_state = jnp.einsum("the,thd->hed", v_blk, k_blk, preferred_element_type=jnp.float32)
    flat = local_state.reshape(HEADS * DK, DK).astype(jnp.float16)
    half = HEADS * DK // 2
    to_second = lax.ppermute(flat[half:], "core", [(0, 1)])
    to_first = lax.ppermute(flat[:half], "core", [(1, 0)])
    first = core == 0
    own = jnp.where(first, flat[:half], flat[half:]).astype(jnp.float32)
    partner = (to_first + to_second).astype(jnp.float32)
    chip_sum = own + partner
    received = lax.all_to_all(chip_sum.astype(jnp.float16), "chip", split_axis=0, concat_axis=0, tiled=True)
    received = received.reshape(chips, half // chips, DK).astype(jnp.float32)
    earlier = jnp.cumsum(received, axis=0) - received
    bound = (chips - 1) * 2 * tok * LIMIT * LIMIT
    shift = max(0, math.ceil(math.log2(bound / F16_MAX)))
    down = np.float32(2.0 ** -shift)
    back = lax.all_to_all((earlier * down).astype(jnp.float16), "chip", split_axis=0, concat_axis=0, tiled=True)
    chip_prefix = back.reshape(half, DK).astype(jnp.float32) * np.float32(2.0 ** shift)
    kept = (chip_prefix + jnp.where(first, jnp.float32(0.0), partner)).astype(jnp.bfloat16)
    sent = (chip_prefix + jnp.where(first, own, jnp.float32(0.0))).astype(jnp.bfloat16)
    rows = lax.broadcasted_iota(jnp.int32, (tok, tok), 0)
    cols = lax.broadcasted_iota(jnp.int32, (tok, tok), 1)
    causal = cols <= rows
    scores = jnp.einsum("thd,shd->hts", q_blk, k_blk, preferred_element_type=jnp.float32)
    scores = jnp.where(causal[None], scores, jnp.float32(0.0)).astype(jnp.bfloat16)
    intra = jnp.einsum("hts,she->the", scores, v_blk, preferred_element_type=jnp.float32)
    sent, intra = lax.optimization_barrier((sent, intra))
    got = swap_cores(sent)
    low = jnp.where(first, kept, got)
    high = jnp.where(first, got, kept)
    carried = jnp.concatenate([low, high], axis=0).reshape(HEADS, DK, DK)
    inter = jnp.einsum("thd,hed->the", q_blk, carried, preferred_element_type=jnp.float32)
    scale = 1.0 / jnp.sqrt(jnp.float32(DK * tok * sources))
    attended = ((intra + inter) * scale).astype(jnp.bfloat16)
    return attended.reshape(tok, HEADS * DK)


def solution(mesh):
    devices = mesh.devices
    split = Mesh(devices.reshape(devices.shape[0], devices.shape[1] // 2, 2), ("groups", "chip", "core"))
    spec = P(("groups", "chip", "core"), None)
    return jax.shard_map(
        on_device, mesh=split, in_specs=(spec, spec, spec), out_specs=spec, check_vma=False
    )
```

```python
import math

import jax
import jax.numpy as jnp
import numpy as np
from jax import lax
from jax.experimental.layout import Layout, with_layout_constraint
from jax.sharding import Mesh
from jax.sharding import PartitionSpec as P

HEADS = 16
DK = 128
LIMIT = 6.0
F16_MAX = 65504.0


def swap_cores(x):
    return lax.ppermute(x, "core", [(0, 1), (1, 0)])


def on_device(queries, keys, values):
    tok = queries.shape[0]
    chips = lax.axis_size("chip")
    core = lax.axis_index("core")
    sources = chips * lax.axis_size("core")
    q_blk = queries.reshape(tok, HEADS, DK)
    k_blk = keys.reshape(tok, HEADS, DK)
    v_blk = values.reshape(tok, HEADS, DK)
    local_state = jnp.einsum("the,thd->hed", v_blk, k_blk, preferred_element_type=jnp.float32)
    flat = local_state.reshape(HEADS * DK, DK).astype(jnp.float16)
    half = HEADS * DK // 2
    partner_all = swap_cores(flat)
    own = lax.dynamic_slice_in_dim(flat, core * half, half).astype(jnp.float32)
    partner = lax.dynamic_slice_in_dim(partner_all, core * half, half).astype(jnp.float32)
    chip_sum = own + partner
    received = lax.all_to_all(chip_sum.astype(jnp.float16), "chip", split_axis=0, concat_axis=0, tiled=True)
    received = received.reshape(chips, half // chips, DK).astype(jnp.float32)
    earlier = jnp.cumsum(received, axis=0) - received
    bound = (chips - 1) * 2 * tok * LIMIT * LIMIT
    shift = max(0, math.ceil(math.log2(bound / F16_MAX)))
    down = np.float32(2.0 ** -shift)
    back = lax.all_to_all((earlier * down).astype(jnp.float16), "chip", split_axis=0, concat_axis=0, tiled=True)
    chip_prefix = back.reshape(half, DK).astype(jnp.float32) * np.float32(2.0 ** shift)
    first = core == 0
    kept = (chip_prefix + jnp.where(first, jnp.float32(0.0), partner)).astype(jnp.bfloat16)
    sent = (chip_prefix + jnp.where(first, own, jnp.float32(0.0))).astype(jnp.bfloat16)
    rows = lax.broadcasted_iota(jnp.int32, (tok, tok), 0)
    cols = lax.broadcasted_iota(jnp.int32, (tok, tok), 1)
    causal = cols <= rows
    scores = jnp.einsum("thd,shd->hts", q_blk, k_blk, preferred_element_type=jnp.float32)
    scores = jnp.where(causal[None], scores, jnp.float32(0.0)).astype(jnp.bfloat16)
    intra = jnp.einsum("hts,she->hte", scores, v_blk, preferred_element_type=jnp.float32)
    intra = with_layout_constraint(intra, Layout(major_to_minor=(0, 2, 1)))
    sent, intra = lax.optimization_barrier((sent, intra))
    got = swap_cores(sent)
    low = jnp.where(first, kept, got)
    high = jnp.where(first, got, kept)
    carried = jnp.concatenate([low, high], axis=0).reshape(HEADS, DK, DK)
    inter = jnp.einsum("thd,hed->hte", q_blk, carried, preferred_element_type=jnp.float32)
    scale = 1.0 / jnp.sqrt(jnp.float32(DK * tok * sources))
    attended = jnp.transpose(((intra + inter) * scale).astype(jnp.bfloat16), (1, 0, 2))
    return attended.reshape(tok, HEADS * DK)


def solution(mesh):
    devices = mesh.devices
    split = Mesh(devices.reshape(devices.shape[0], devices.shape[1] // 2, 2), ("groups", "chip", "core"))
    spec = P(("groups", "chip", "core"), None)
    return jax.shard_map(
        on_device, mesh=split, in_specs=(spec, spec, spec), out_specs=spec, check_vma=False
    )
```

```python
import math

import jax
import jax.numpy as jnp
import numpy as np
from jax import lax
from jax.sharding import Mesh
from jax.sharding import PartitionSpec as P

HEADS = 16
DK = 128
LIMIT = 6.0
F16_MAX = 65504.0


def swap_cores(x):
    return lax.ppermute(x, "core", [(0, 1), (1, 0)])


def on_device(queries, keys, values):
    tok = queries.shape[0]
    chips = lax.axis_size("chip")
    core = lax.axis_index("core")
    sources = chips * lax.axis_size("core")
    q_blk = queries.reshape(tok, HEADS, DK)
    k_blk = keys.reshape(tok, HEADS, DK)
    v_blk = values.reshape(tok, HEADS, DK)
    local_state = jnp.einsum("the,thd->hed", v_blk, k_blk, preferred_element_type=jnp.float32)
    flat = local_state.reshape(HEADS * DK, DK).astype(jnp.float16)
    half = HEADS * DK // 2
    first = core == 0
    low, high = flat[:half], flat[half:]
    partner = swap_cores(jnp.where(first, high, low)).astype(jnp.float32)
    own = jnp.where(first, low, high).astype(jnp.float32)
    chip_sum = own + partner
    received = lax.all_to_all(chip_sum.astype(jnp.float16), "chip", split_axis=0, concat_axis=0, tiled=True)
    received = received.reshape(chips, half // chips, DK).astype(jnp.float32)
    earlier = jnp.cumsum(received, axis=0) - received
    bound = (chips - 1) * 2 * tok * LIMIT * LIMIT
    shift = max(0, math.ceil(math.log2(bound / F16_MAX)))
    down = np.float32(2.0 ** -shift)
    back = lax.all_to_all((earlier * down).astype(jnp.float16), "chip", split_axis=0, concat_axis=0, tiled=True)
    chip_prefix = back.reshape(half, DK).astype(jnp.float32) * np.float32(2.0 ** shift)
    kept = (chip_prefix + jnp.where(first, jnp.float32(0.0), partner)).astype(jnp.bfloat16)
    sent = (chip_prefix + jnp.where(first, own, jnp.float32(0.0))).astype(jnp.bfloat16)
    rows = lax.broadcasted_iota(jnp.int32, (tok, tok), 0)
    cols = lax.broadcasted_iota(jnp.int32, (tok, tok), 1)
    causal = cols <= rows
    scores = jnp.einsum("thd,shd->hts", q_blk, k_blk, preferred_element_type=jnp.float32)
    scores = jnp.where(causal[None], scores, jnp.float32(0.0)).astype(jnp.bfloat16)
    intra = jnp.einsum("hts,she->the", scores, v_blk, preferred_element_type=jnp.float32)
    sent, intra = lax.optimization_barrier((sent, intra))
    got = swap_cores(sent)
    carried = jnp.concatenate([jnp.where(first, kept, got), jnp.where(first, got, kept)], axis=0).reshape(HEADS, DK, DK)
    inter = jnp.einsum("thd,hed->the", q_blk, carried, preferred_element_type=jnp.float32)
    scale = 1.0 / jnp.sqrt(jnp.float32(DK * tok * sources))
    attended = ((intra + inter) * scale).astype(jnp.bfloat16)
    return attended.reshape(tok, HEADS * DK)


def solution(mesh):
    devices = mesh.devices
    split = Mesh(devices.reshape(devices.shape[0], devices.shape[1] // 2, 2), ("groups", "chip", "core"))
    spec = P(("groups", "chip", "core"), None)
    return jax.shard_map(
        on_device, mesh=split, in_specs=(spec, spec, spec), out_specs=spec, check_vma=False
    )
```

```python
import functools
import math

import jax
import jax.numpy as jnp
import numpy as np
from jax import lax
from jax.experimental import pallas as pl
from jax.experimental.pallas import tpu as pltpu
from jax.sharding import Mesh
from jax.sharding import PartitionSpec as P

HEADS = 16
DK = 128
LIMIT = 6.0
F16_MAX = 65504.0


def combine_kernel(scale, q_ref, p_ref, intra_ref, o_ref):
    for h in range(HEADS):
        cols = slice(h * DK, (h + 1) * DK)
        inter = lax.dot_general(
            q_ref[:, cols], p_ref[h * DK:(h + 1) * DK, :], (((1,), (1,)), ((), ())),
            preferred_element_type=jnp.float32,
        )
        o_ref[:, cols] = ((intra_ref[h] + inter) * scale).astype(o_ref.dtype)


def combine(queries, carried_t, intra, scale):
    tok = queries.shape[0]
    whole = pl.BlockSpec(memory_space=pltpu.VMEM)
    return pl.pallas_call(
        functools.partial(combine_kernel, scale),
        in_specs=[whole] * 3,
        out_specs=whole,
        out_shape=jax.ShapeDtypeStruct((tok, HEADS * DK), jnp.bfloat16),
        cost_estimate=pl.CostEstimate(
            flops=2 * tok * DK * DK * HEADS, transcendentals=0,
            bytes_accessed=2 * tok * HEADS * DK * 2 + tok * HEADS * DK * 4 + HEADS * DK * DK * 2,
        ),
    )(queries, carried_t, intra)


def swap_cores(x):
    return lax.ppermute(x, "core", [(0, 1), (1, 0)])


def on_device(queries, keys, values):
    tok = queries.shape[0]
    chips = lax.axis_size("chip")
    core = lax.axis_index("core")
    sources = chips * lax.axis_size("core")
    q_blk = queries.reshape(tok, HEADS, DK)
    k_blk = keys.reshape(tok, HEADS, DK)
    v_blk = values.reshape(tok, HEADS, DK)
    local_state = jnp.einsum("the,thd->hed", v_blk, k_blk, preferred_element_type=jnp.float32)
    flat = local_state.reshape(HEADS * DK, DK).astype(jnp.float16)
    half = HEADS * DK // 2
    first = core == 0
    low, high = flat[:half], flat[half:]
    partner = swap_cores(jnp.where(first, high, low)).astype(jnp.float32)
    own = jnp.where(first, low, high).astype(jnp.float32)
    chip_sum = own + partner
    received = lax.all_to_all(chip_sum.astype(jnp.float16), "chip", split_axis=0, concat_axis=0, tiled=True)
    received = received.reshape(chips, half // chips, DK).astype(jnp.float32)
    earlier = jnp.cumsum(received, axis=0) - received
    bound = (chips - 1) * 2 * tok * LIMIT * LIMIT
    shift = max(0, math.ceil(math.log2(bound / F16_MAX)))
    down = np.float32(2.0 ** -shift)
    back = lax.all_to_all((earlier * down).astype(jnp.float16), "chip", split_axis=0, concat_axis=0, tiled=True)
    chip_prefix = back.reshape(half, DK).astype(jnp.float32) * np.float32(2.0 ** shift)
    kept = (chip_prefix + jnp.where(first, jnp.float32(0.0), partner)).astype(jnp.bfloat16)
    sent = (chip_prefix + jnp.where(first, own, jnp.float32(0.0))).astype(jnp.bfloat16)
    rows = lax.broadcasted_iota(jnp.int32, (tok, tok), 0)
    cols = lax.broadcasted_iota(jnp.int32, (tok, tok), 1)
    causal = cols <= rows
    scores = jnp.einsum("thd,shd->hts", q_blk, k_blk, preferred_element_type=jnp.float32)
    scores = jnp.where(causal[None], scores, jnp.float32(0.0)).astype(jnp.bfloat16)
    intra = jnp.einsum("hts,she->hte", scores, v_blk, preferred_element_type=jnp.float32)
    sent, intra = lax.optimization_barrier((sent, intra))
    got = swap_cores(sent)
    carried_t = jnp.concatenate([jnp.where(first, kept, got), jnp.where(first, got, kept)], axis=0)
    scale = float(np.float32(1.0) / np.sqrt(np.float32(DK * tok * sources)))
    return combine(queries, carried_t, intra, scale)

def solution(mesh):
    devices = mesh.devices
    split = Mesh(devices.reshape(devices.shape[0], devices.shape[1] // 2, 2), ("groups", "chip", "core"))
    spec = P(("groups", "chip", "core"), None)
    return jax.shard_map(
        on_device, mesh=split, in_specs=(spec, spec, spec), out_specs=spec, check_vma=False
    )
```

```python
import math

import jax
import jax.numpy as jnp
import numpy as np
from jax import lax
from jax.sharding import Mesh
from jax.sharding import PartitionSpec as P

HEADS = 16
DK = 128
LIMIT = 6.0
F16_MAX = 65504.0


def swap_cores(x):
    return lax.ppermute(x, "core", [(0, 1), (1, 0)])


def on_device(queries, keys, values):
    tok = queries.shape[0]
    chips = lax.axis_size("chip")
    core = lax.axis_index("core")
    sources = chips * lax.axis_size("core")
    q_blk = queries.reshape(tok, HEADS, DK)
    k_blk = keys.reshape(tok, HEADS, DK)
    v_blk = values.reshape(tok, HEADS, DK)
    local_state = jnp.einsum("the,thd->hed", v_blk, k_blk, preferred_element_type=jnp.float32)
    flat = local_state.reshape(HEADS * DK, DK).astype(jnp.float16)
    half = HEADS * DK // 2
    first = core == 0
    low, high = flat[:half], flat[half:]
    partner = swap_cores(jnp.where(first, high, low)).astype(jnp.float32)
    own = jnp.where(first, low, high).astype(jnp.float32)
    chip_sum = own + partner
    received = lax.all_to_all(chip_sum.astype(jnp.float16), "chip", split_axis=0, concat_axis=0, tiled=True)
    received, keys_late, values_late = lax.optimization_barrier((received, keys, values))
    received = received.reshape(chips, half // chips, DK).astype(jnp.float32)
    earlier = jnp.cumsum(received, axis=0) - received
    bound = (chips - 1) * 2 * tok * LIMIT * LIMIT
    shift = max(0, math.ceil(math.log2(bound / F16_MAX)))
    down = np.float32(2.0 ** -shift)
    back = lax.all_to_all((earlier * down).astype(jnp.float16), "chip", split_axis=0, concat_axis=0, tiled=True)
    chip_prefix = back.reshape(half, DK).astype(jnp.float32) * np.float32(2.0 ** shift)
    kept = (chip_prefix + jnp.where(first, jnp.float32(0.0), partner)).astype(jnp.bfloat16)
    sent = (chip_prefix + jnp.where(first, own, jnp.float32(0.0))).astype(jnp.bfloat16)
    rows = lax.broadcasted_iota(jnp.int32, (tok, tok), 0)
    cols = lax.broadcasted_iota(jnp.int32, (tok, tok), 1)
    causal = cols <= rows
    scores = jnp.einsum("thd,shd->hts", q_blk, keys_late.reshape(tok, HEADS, DK), preferred_element_type=jnp.float32)
    scores = jnp.where(causal[None], scores, jnp.float32(0.0)).astype(jnp.bfloat16)
    intra = jnp.einsum("hts,she->het", scores, values_late.reshape(tok, HEADS, DK), preferred_element_type=jnp.float32)
    sent, intra = lax.optimization_barrier((sent, intra.reshape(HEADS * DK, tok)))
    intra = jnp.transpose(intra.reshape(HEADS, DK, tok), (2, 0, 1))
    got = swap_cores(sent)
    carried = jnp.concatenate([jnp.where(first, kept, got), jnp.where(first, got, kept)], axis=0).reshape(HEADS, DK, DK)
    inter = jnp.einsum("thd,hed->the", q_blk, carried, preferred_element_type=jnp.float32)
    scale = 1.0 / jnp.sqrt(jnp.float32(DK * tok * sources))
    attended = ((intra + inter) * scale).astype(jnp.bfloat16)
    return attended.reshape(tok, HEADS * DK)


def solution(mesh):
    devices = mesh.devices
    split = Mesh(devices.reshape(devices.shape[0], devices.shape[1] // 2, 2), ("groups", "chip", "core"))
    spec = P(("groups", "chip", "core"), None)
    return jax.shard_map(
        on_device, mesh=split, in_specs=(spec, spec, spec), out_specs=spec, check_vma=False
    )
```

```python
import math

import jax
import jax.numpy as jnp
import numpy as np
from jax import lax
from jax.sharding import Mesh
from jax.sharding import PartitionSpec as P

HEADS = 16
DK = 128
LIMIT = 6.0
F16_MAX = 65504.0


def swap_cores(x):
    return lax.ppermute(x, "core", [(0, 1), (1, 0)])


def on_device(queries, keys, values):
    tok = queries.shape[0]
    chips = lax.axis_size("chip")
    core = lax.axis_index("core")
    sources = chips * lax.axis_size("core")
    q_blk = queries.reshape(tok, HEADS, DK)
    k_blk = keys.reshape(tok, HEADS, DK)
    v_blk = values.reshape(tok, HEADS, DK)
    local_state = jnp.einsum("thd,the->hde", k_blk, v_blk, preferred_element_type=jnp.float32)
    flat = local_state.reshape(HEADS * DK, DK).astype(jnp.float16)
    half = HEADS * DK // 2
    first = core == 0
    low, high = flat[:half], flat[half:]
    partner = swap_cores(jnp.where(first, high, low)).astype(jnp.float32)
    own = jnp.where(first, low, high).astype(jnp.float32)
    chip_sum = own + partner
    received = lax.all_to_all(chip_sum.astype(jnp.float16), "chip", split_axis=0, concat_axis=0, tiled=True)
    received, keys_late, values_late = lax.optimization_barrier((received, keys, values))
    received = received.reshape(chips, half // chips, DK).astype(jnp.float32)
    earlier = jnp.cumsum(received, axis=0) - received
    bound = (chips - 1) * 2 * tok * LIMIT * LIMIT
    shift = max(0, math.ceil(math.log2(bound / F16_MAX)))
    down = np.float32(2.0 ** -shift)
    back = lax.all_to_all((earlier * down).astype(jnp.float16), "chip", split_axis=0, concat_axis=0, tiled=True)
    chip_prefix = back.reshape(half, DK).astype(jnp.float32) * np.float32(2.0 ** shift)
    kept = (chip_prefix + jnp.where(first, jnp.float32(0.0), partner)).astype(jnp.bfloat16)
    sent = (chip_prefix + jnp.where(first, own, jnp.float32(0.0))).astype(jnp.bfloat16)
    rows = lax.broadcasted_iota(jnp.int32, (tok, tok), 0)
    cols = lax.broadcasted_iota(jnp.int32, (tok, tok), 1)
    causal = cols <= rows
    scores = jnp.einsum("thd,shd->hts", q_blk, keys_late.reshape(tok, HEADS, DK), preferred_element_type=jnp.float32)
    scores = jnp.where(causal[None], scores, jnp.float32(0.0)).astype(jnp.bfloat16)
    intra = jnp.einsum("hts,she->het", scores, values_late.reshape(tok, HEADS, DK), preferred_element_type=jnp.float32)
    sent, intra = lax.optimization_barrier((sent, intra.reshape(HEADS * DK, tok)))
    intra = jnp.transpose(intra.reshape(HEADS, DK, tok), (2, 0, 1))
    got = swap_cores(sent)
    carried = jnp.concatenate([jnp.where(first, kept, got), jnp.where(first, got, kept)], axis=0).reshape(HEADS, DK, DK)
    inter = jnp.einsum("thd,hde->the", q_blk, carried, preferred_element_type=jnp.float32)
    scale = 1.0 / jnp.sqrt(jnp.float32(DK * tok * sources))
    attended = ((intra + inter) * scale).astype(jnp.bfloat16)
    return attended.reshape(tok, HEADS * DK)


def solution(mesh):
    devices = mesh.devices
    split = Mesh(devices.reshape(devices.shape[0], devices.shape[1] // 2, 2), ("groups", "chip", "core"))
    spec = P(("groups", "chip", "core"), None)
    return jax.shard_map(
        on_device, mesh=split, in_specs=(spec, spec, spec), out_specs=spec, check_vma=False
    )
```
